512 devices in a mesh: row: 32 (over z, x_hi), col: 16 (over y, x_lo, core).
Axes of the slice: x: 4 (x_hi: 2, x_lo: 2; x = x_hi * 2 + x_lo), y: 4, z: 16, core: 2. Of those that a mesh axis runs over, the one named last changes fastest.
Arguments:
- features: bfloat16 [48, 2048, 2048], P(None, 'row', 'col'), may hold values from -6 to 6
- w_dilated: bfloat16 [2, 3, 3, 48, 48], replicated, may hold values from -0.3125 to 0.3125
- w_pointwise: bfloat16 [2, 48, 48], replicated, may hold values from -0.875 to 0.875
- norm_gain: float32 [2, 2, 48], replicated, may hold values from 0.25 to 1.75
- norm_bias: float32 [2, 2, 48], replicated, may hold values from -0.5 to 0.5
Outputs:
- refined: bfloat16 [48, 2048, 2048], P(None, 'row', 'col')
The draws below stay inside these ranges and needn't reach their ends.
All inputs are finite; a program needn't handle non-finite values.
Results may differ from the reference program's by a relative error of at most 0.0065.
Values may be sent and summed in bfloat16 or wider, within the bound.
No kernel may reach another device: no remote copies, remote signals or barrier semaphores. Data moves between devices by JAX's collectives and lax.ppermute only.
A program may use at most 64 MiB of HBM per device.

```python
import jax
import jax.numpy as jnp
from jax import lax

CH = 48
FIRST_DILATION = 8
SECOND_DILATION = 16
TR = 64
N = 2048


def level_of(rng, dims, pieces, least, largest):
    def one(axis_at, shards_of):
        heights = jax.random.uniform(jax.random.fold_in(jax.random.fold_in(rng, 6), axis_at), (shards_of,), jnp.float32, least / len(pieces), largest / len(pieces))
        return jnp.repeat(jnp.exp(heights), dims[axis_at] // shards_of).reshape((-1,) + (1,) * (len(dims) - axis_at - 1))

    gain = one(*pieces[0])
    for cut in pieces[1:]:
        gain = gain * one(*cut)
    return gain


def gaussian(rng, extent, width, reach, pieces=(), held_as=jnp.bfloat16):
    level = level_of(rng, extent, pieces, -0.22, 0.18) if pieces else 1.0
    values = jax.random.normal(rng, extent, jnp.float32) * width * level
    return jnp.minimum(jnp.maximum(values, -reach), reach).astype(held_as)


def setup_inputs(seed: int = 0) -> dict:
    streams_of = jax.random.split(jax.random.key(seed), 6)
    return {
        "features": gaussian(streams_of[0], (CH, N, N), 1.0, 6.0, ((1, 32), (2, 16))),
        "w_dilated": gaussian(streams_of[1], (2, 3, 3, CH, CH), (9 * CH) ** -0.5, 0.3125),
        "w_pointwise": gaussian(streams_of[2], (2, CH, CH), CH ** -0.5, 0.875),
        "norm_gain": jnp.clip(1.0 + 0.15 * jax.random.normal(streams_of[3], (2, 2, CH), jnp.float32), 0.25, 1.75),
        "norm_bias": jnp.clip(jax.random.uniform(streams_of[4], (2, 2, CH), jnp.float32, -0.5, 0.5), -0.5, 0.5),
    }


def dilated_terms(segment, kernel, gain_pair, bias_pair, pointwise, dilation_rate):
    active = jnp.maximum(segment.astype(jnp.float32), 0.0)
    spread = lax.conv_general_dilated(active[None], kernel.astype(jnp.float32), (1, 1), "VALID", rhs_dilation=(dilation_rate, dilation_rate), precision=lax.Precision.HIGHEST)[0]
    hidden = jnp.maximum(spread * gain_pair[0][:, None, None] + bias_pair[0][:, None, None], 0.0).astype(jnp.bfloat16)
    branch = jnp.einsum("oc,chw->ohw", pointwise.astype(jnp.float32), hidden.astype(jnp.float32), precision=lax.Precision.HIGHEST)
    return branch * gain_pair[1][:, None, None] + bias_pair[1][:, None, None]


def residual_block(current_state, kernel, gain_pair, bias_pair, pointwise, dilation_rate):
    height = TR
    strips = N // height
    anchor = jnp.zeros((), jnp.int32)
    padded = jnp.pad(current_state, ((0, 0), (dilation_rate, dilation_rate), (dilation_rate, dilation_rate)))

    def strip_block(position_index):
        offset = (position_index * height).astype(jnp.int32)
        segment = lax.dynamic_slice(padded, (anchor, offset, anchor), (CH, height + 2 * dilation_rate, N + 2 * dilation_rate))
        own_rows = lax.dynamic_slice(current_state, (anchor, offset, anchor), (CH, height, N))
        terms = dilated_terms(segment, kernel, gain_pair, bias_pair, pointwise, dilation_rate)
        return (own_rows.astype(jnp.float32) + terms).astype(jnp.bfloat16)

    stacked = lax.map(strip_block, jnp.arange(strips, dtype=jnp.int32))
    output_map = jnp.transpose(stacked, (1, 0, 2, 3)).reshape(CH, N, N)
    output_map = lax.optimization_barrier(output_map)

    def symmetrize(position_index):
        offset = (position_index * height).astype(jnp.int32)
        row_part = lax.dynamic_slice(output_map, (anchor, offset, anchor), (CH, height, N)).astype(jnp.float32)
        col_part = lax.dynamic_slice(output_map, (anchor, anchor, offset), (CH, N, height)).astype(jnp.float32)
        return ((row_part + jnp.swapaxes(col_part, 1, 2)) * 0.5).astype(jnp.bfloat16)

    halves = lax.map(symmetrize, jnp.arange(strips, dtype=jnp.int32))
    return jnp.transpose(halves, (1, 0, 2, 3)).reshape(CH, N, N)


def reference(features, w_dilated, w_pointwise, norm_gain, norm_bias):
    current_state = features
    for layer_index in range(2):
        dilation_rate = FIRST_DILATION if layer_index == 0 else SECOND_DILATION
        kernel = jnp.transpose(w_dilated[layer_index], (2, 3, 0, 1))
        current_state = residual_block(current_state, kernel, norm_gain[layer_index], norm_bias[layer_index], w_pointwise[layer_index], dilation_rate)
    return current_state
```

```python
import jax
import jax.numpy as jnp
from jax import lax
from jax.sharding import PartitionSpec as P

FIRST_DILATION = 8
SECOND_DILATION = 16


def padded(value, sides, width):
    for axis, dim in sides:
        size, length = (lax.axis_size(axis), value.shape[dim])
        up = [(i, (i + 1) % size) for i in range(size - 1)]
        down = [(j, i) for i, j in up]
        last = lax.slice_in_dim(value, length - width, length, axis=dim)
        initial = lax.slice_in_dim(value, 0, width, axis=dim)
        before = lax.ppermute(last, axis, up)
        after = lax.ppermute(initial, axis, down)
        value = jnp.concatenate([before, value, after], axis=dim)
    return value


def dilated_terms(
    extended_input, current_state, kernel, gain_pair, bias_pair, pointwise, dilation_rate
):
    active = jnp.maximum(extended_input, jnp.zeros((), extended_input.dtype))
    spread = lax.conv_general_dilated(
        active[None],
        kernel,
        (1, 1),
        "VALID",
        rhs_dilation=(dilation_rate, dilation_rate),
        preferred_element_type=jnp.float32,
    )[0]
    hidden = jnp.maximum(
        spread * gain_pair[0][:, None, None] + bias_pair[0][:, None, None], 0.0
    ).astype(jnp.bfloat16)
    branch = jnp.einsum("oc,chw->ohw", pointwise, hidden, preferred_element_type=jnp.float32)
    summed = (
        current_state.astype(jnp.float32)
        + branch * gain_pair[1][:, None, None]
        + bias_pair[1][:, None, None]
    )
    return summed.astype(jnp.bfloat16)


def mirror_pieces(output_map):
    n_row = lax.axis_size("row")
    n_col = lax.axis_size("col")
    channel_count, tile_rows, tile_cols = output_map.shape
    k = tile_cols // tile_rows
    parity = lax.axis_index("row") % k
    flipped = jnp.swapaxes(output_map, 1, 2)
    received = []
    for m in range(k):
        piece = lax.dynamic_slice_in_dim(flipped, ((parity + m) % k) * tile_rows, tile_rows, axis=1)
        pairs = []
        for r in range(n_row):
            for c in range(n_col):
                h = (r % k + m) % k
                pairs.append((r * n_col + c, (k * c + h) * n_col + r // k))
        received.append(lax.ppermute(piece, ("row", "col"), pairs))
    return [lax.select_n((parity - s) % k, *received) if k > 1 else received[0] for s in range(k)]


def symmetrized(output_map):
    pieces = mirror_pieces(output_map)
    tile_rows = output_map.shape[1]
    halves = []
    for s, piece in enumerate(pieces):
        own = output_map[:, :, s * tile_rows:(s + 1) * tile_rows]
        halves.append(((own.astype(jnp.float32) + piece.astype(jnp.float32)) * 0.5).astype(jnp.bfloat16))
    return jnp.concatenate(halves, axis=2)


def body(features, w_dilated, w_pointwise, norm_gain, norm_bias):
    current_state = features
    for layer_index in range(2):
        dilation_rate = FIRST_DILATION if layer_index == 0 else SECOND_DILATION
        extended_input = padded(current_state, (("row", 1), ("col", 2)), dilation_rate)
        kernel = jnp.transpose(w_dilated[layer_index], (2, 3, 0, 1))
        output_map = dilated_terms(
            extended_input,
            current_state,
            kernel,
            norm_gain[layer_index],
            norm_bias[layer_index],
            w_pointwise[layer_index],
            dilation_rate,
        )
        current_state = symmetrized(output_map)
    return current_state


def solution(mesh):
    in_specs = (P(None, "row", "col"), P(), P(), P(), P())
    out_specs = P(None, "row", "col")
    return jax.shard_map(body, mesh=mesh, in_specs=in_specs, out_specs=out_specs, check_vma=False)
```

```python
import jax
import jax.numpy as jnp
from jax import lax
from jax.sharding import PartitionSpec as P

FIRST_DILATION = 8
SECOND_DILATION = 16


def padded(value, sides, width):
    for axis, dim in sides:
        size, length = (lax.axis_size(axis), value.shape[dim])
        up = [(i, (i + 1) % size) for i in range(size - 1)]
        down = [(j, i) for i, j in up]
        last = lax.slice_in_dim(value, length - width, length, axis=dim)
        initial = lax.slice_in_dim(value, 0, width, axis=dim)
        before = lax.ppermute(last, axis, up)
        after = lax.ppermute(initial, axis, down)
        value = jnp.concatenate([before, value, after], axis=dim)
    return value


def hidden_of(extended_input, kernel, gain, bias, dilation_rate):
    active = jnp.maximum(extended_input, jnp.zeros((), extended_input.dtype))
    spread = lax.conv_general_dilated(
        active[None],
        kernel,
        (1, 1),
        "VALID",
        rhs_dilation=(dilation_rate, dilation_rate),
        preferred_element_type=jnp.float32,
    )[0]
    return jnp.maximum(spread * gain[:, None, None] + bias[:, None, None], 0.0).astype(jnp.bfloat16)


def block_output(current_state, hidden, gain_pair, bias_pair, pointwise):
    branch = jnp.einsum("oc,chw->ohw", pointwise, hidden, preferred_element_type=jnp.float32)
    summed = (
        current_state.astype(jnp.float32)
        + branch * gain_pair[1][:, None, None]
        + bias_pair[1][:, None, None]
    )
    return summed.astype(jnp.bfloat16)


def mirror_tile(output_map):
    n_row = lax.axis_size("row")
    n_col = lax.axis_size("col")
    channel_count, tile_rows, tile_cols = output_map.shape
    sub_rows = tile_rows // n_col
    ratio = n_row // n_col
    first_leg = lax.all_to_all(output_map, "col", split_axis=1, concat_axis=2, tiled=True)
    count = first_leg.shape[0]
    moved = lax.all_to_all(
        lax.all_to_all(first_leg, "row", split_axis=2, concat_axis=1, tiled=True),
        "col",
        split_axis=1,
        concat_axis=1,
        tiled=True,
    )
    grouped = moved.reshape(count, n_col, ratio, sub_rows, tile_rows)
    return jnp.transpose(grouped, (0, 4, 2, 1, 3)).reshape(count, tile_rows, tile_cols)


def mean_of(a, b):
    return ((a.astype(jnp.float32) + b.astype(jnp.float32)) * 0.5).astype(jnp.bfloat16)


def body(features, w_dilated, w_pointwise, norm_gain, norm_bias):
    kernel = jnp.transpose(w_dilated[0], (2, 3, 0, 1))
    extended = padded(features, (("row", 1), ("col", 2)), FIRST_DILATION)
    hidden = hidden_of(extended, kernel, norm_gain[0, 0], norm_bias[0, 0], FIRST_DILATION)
    output_map = block_output(features, hidden, norm_gain[0], norm_bias[0], w_pointwise[0])
    state = mean_of(output_map, mirror_tile(output_map))

    kernel = jnp.transpose(w_dilated[1], (2, 3, 0, 1))
    both = jnp.concatenate([kernel, jnp.swapaxes(kernel, 2, 3)], axis=0)
    extended = padded(state, (("row", 1), ("col", 2)), SECOND_DILATION)
    gain = jnp.concatenate([norm_gain[1, 0], norm_gain[1, 0]])
    bias = jnp.concatenate([norm_bias[1, 0], norm_bias[1, 0]])
    hidden = hidden_of(extended, both, gain, bias, SECOND_DILATION)
    count = state.shape[0]
    direct = block_output(state, hidden[:count], norm_gain[1], norm_bias[1], w_pointwise[1])
    mirrored = block_output(state, hidden[count:], norm_gain[1], norm_bias[1], w_pointwise[1])
    return mean_of(direct, mirrored)


def solution(mesh):
    in_specs = (P(None, "row", "col"), P(), P(), P(), P())
    out_specs = P(None, "row", "col")
    return jax.shard_map(body, mesh=mesh, in_specs=in_specs, out_specs=out_specs, check_vma=False)
```

```python
import jax
import jax.numpy as jnp
from jax import lax
from jax.sharding import PartitionSpec as P

FIRST_DILATION = 8
SECOND_DILATION = 16


def padded(value, sides, width):
    for axis, dim in sides:
        size, length = (lax.axis_size(axis), value.shape[dim])
        up = [(i, (i + 1) % size) for i in range(size - 1)]
        down = [(j, i) for i, j in up]
        last = lax.slice_in_dim(value, length - width, length, axis=dim)
        initial = lax.slice_in_dim(value, 0, width, axis=dim)
        before = lax.ppermute(last, axis, up)
        after = lax.ppermute(initial, axis, down)
        value = jnp.concatenate([before, value, after], axis=dim)
    return value


def hidden_of(extended_input, kernel, gain, bias, dilation_rate, tile_rows, tile_cols):
    active = jnp.maximum(extended_input, jnp.zeros((), extended_input.dtype))
    windows = [
        lax.slice(
            active,
            (0, p * dilation_rate, q * dilation_rate),
            (active.shape[0], p * dilation_rate + tile_rows, q * dilation_rate + tile_cols),
        )
        for p in range(3)
        for q in range(3)
    ]
    stacked = jnp.stack(windows, axis=0)
    spread = jnp.einsum("toc,tchw->ohw", kernel, stacked, preferred_element_type=jnp.float32)
    hidden = jnp.maximum(spread * gain[:, None, None] + bias[:, None, None], 0.0)
    return hidden.astype(jnp.bfloat16)


def block_output(current_state, hidden, gain_pair, bias_pair, pointwise):
    branch = jnp.einsum("oc,chw->ohw", pointwise, hidden, preferred_element_type=jnp.float32)
    summed = (
        current_state.astype(jnp.float32)
        + branch * gain_pair[1][:, None, None]
        + bias_pair[1][:, None, None]
    )
    return lax.reduce_precision(summed, exponent_bits=8, mantissa_bits=7).astype(jnp.bfloat16)


def mirror_tile(output_map):
    n_row = lax.axis_size("row")
    n_col = lax.axis_size("col")
    channel_count, tile_rows, tile_cols = output_map.shape
    sub_rows = tile_rows // n_col
    ratio = n_row // n_col
    first_leg = lax.all_to_all(output_map, "col", split_axis=1, concat_axis=2, tiled=True)
    count = first_leg.shape[0]
    moved = lax.all_to_all(
        lax.all_to_all(first_leg, "row", split_axis=2, concat_axis=1, tiled=True),
        "col",
        split_axis=1,
        concat_axis=1,
        tiled=True,
    )
    grouped = moved.reshape(count, n_col, ratio, sub_rows, tile_rows)
    return jnp.transpose(grouped, (0, 4, 2, 1, 3)).reshape(count, tile_rows, tile_cols)


def mean_of(a, b):
    return ((a.astype(jnp.float32) + b.astype(jnp.float32)) * 0.5).astype(jnp.bfloat16)


def body(features, w_dilated, w_pointwise, norm_gain, norm_bias):
    count, tile_rows, tile_cols = features.shape
    kernel = w_dilated[0].reshape(9, count, count)
    extended = padded(features, (("row", 1), ("col", 2)), FIRST_DILATION)
    hidden = hidden_of(
        extended, kernel, norm_gain[0, 0], norm_bias[0, 0], FIRST_DILATION, tile_rows, tile_cols
    )
    output_map = block_output(features, hidden, norm_gain[0], norm_bias[0], w_pointwise[0])
    state = mean_of(output_map, mirror_tile(output_map))

    kernel = w_dilated[1]
    both = jnp.concatenate([kernel, jnp.swapaxes(kernel, 0, 1)], axis=2).reshape(9, 2 * count, count)
    extended = padded(state, (("row", 1), ("col", 2)), SECOND_DILATION)
    gain = jnp.concatenate([norm_gain[1, 0], norm_gain[1, 0]])
    bias = jnp.concatenate([norm_bias[1, 0], norm_bias[1, 0]])
    hidden = hidden_of(extended, both, gain, bias, SECOND_DILATION, tile_rows, tile_cols)
    direct = block_output(state, hidden[:count], norm_gain[1], norm_bias[1], w_pointwise[1])
    mirrored = block_output(state, hidden[count:], norm_gain[1], norm_bias[1], w_pointwise[1])
    return mean_of(direct, mirrored)


def solution(mesh):
    in_specs = (P(None, "row", "col"), P(), P(), P(), P())
    out_specs = P(None, "row", "col")
    return jax.shard_map(body, mesh=mesh, in_specs=in_specs, out_specs=out_specs, check_vma=False)
```

```python
import jax
import jax.numpy as jnp
from jax import lax
from jax.sharding import PartitionSpec as P

FIRST_DILATION = 8
SECOND_DILATION = 16


def halo(value, width):
    n_row = lax.axis_size("row")
    n_col = lax.axis_size("col")
    rows, cols = value.shape[1], value.shape[2]
    head = slice(0, width)
    tail = slice(rows - width, rows), slice(cols - width, cols)

    def shifted(piece, d_row, d_col):
        pairs = []
        for r in range(n_row):
            for c in range(n_col):
                if 0 <= r + d_row < n_row and 0 <= c + d_col < n_col:
                    pairs.append((r * n_col + c, (r + d_row) * n_col + c + d_col))
        return lax.ppermute(piece, ("row", "col"), pairs)

    all_rows, all_cols = slice(0, rows), slice(0, cols)
    top = shifted(value[:, tail[0], all_cols], 1, 0)
    bottom = shifted(value[:, head, all_cols], -1, 0)
    left = shifted(value[:, all_rows, tail[1]], 0, 1)
    right = shifted(value[:, all_rows, head], 0, -1)
    top_left = shifted(value[:, tail[0], tail[1]], 1, 1)
    top_right = shifted(value[:, tail[0], head], 1, -1)
    bottom_left = shifted(value[:, head, tail[1]], -1, 1)
    bottom_right = shifted(value[:, head, head], -1, -1)
    return jnp.concatenate(
        [
            jnp.concatenate([top_left, top, top_right], axis=2),
            jnp.concatenate([left, value, right], axis=2),
            jnp.concatenate([bottom_left, bottom, bottom_right], axis=2),
        ],
        axis=1,
    )


def hidden_of(extended_input, kernel, gain, bias, dilation_rate, tile_rows, tile_cols):
    active = jnp.maximum(extended_input, jnp.zeros((), extended_input.dtype))
    windows = [
        lax.slice(
            active,
            (0, p * dilation_rate, q * dilation_rate),
            (active.shape[0], p * dilation_rate + tile_rows, q * dilation_rate + tile_cols),
        )
        for p in range(3)
        for q in range(3)
    ]
    stacked = jnp.stack(windows, axis=0)
    spread = jnp.einsum("toc,tchw->ohw", kernel, stacked, preferred_element_type=jnp.float32)
    hidden = jnp.maximum(spread * gain[:, None, None] + bias[:, None, None], 0.0)
    return hidden.astype(jnp.bfloat16)


def block_output(current_state, hidden, gain_pair, bias_pair, pointwise):
    branch = jnp.einsum("oc,chw->ohw", pointwise, hidden, preferred_element_type=jnp.float32)
    summed = (
        current_state.astype(jnp.float32)
        + branch * gain_pair[1][:, None, None]
        + bias_pair[1][:, None, None]
    )
    return lax.reduce_precision(summed, exponent_bits=8, mantissa_bits=7).astype(jnp.bfloat16)


def mirror_tile(output_map):
    n_row = lax.axis_size("row")
    n_col = lax.axis_size("col")
    channel_count, tile_rows, tile_cols = output_map.shape
    sub_rows = tile_rows // n_col
    ratio = n_row // n_col
    first_leg = lax.all_to_all(output_map, "col", split_axis=1, concat_axis=2, tiled=True)
    count = first_leg.shape[0]
    moved = lax.all_to_all(
        lax.all_to_all(first_leg, "row", split_axis=2, concat_axis=1, tiled=True),
        "col",
        split_axis=1,
        concat_axis=1,
        tiled=True,
    )
    grouped = moved.reshape(count, n_col, ratio, sub_rows, tile_rows)
    return jnp.transpose(grouped, (0, 4, 2, 1, 3)).reshape(count, tile_rows, tile_cols)


def mean_of(a, b):
    return ((a.astype(jnp.float32) + b.astype(jnp.float32)) * 0.5).astype(jnp.bfloat16)


def body(features, w_dilated, w_pointwise, norm_gain, norm_bias):
    count, tile_rows, tile_cols = features.shape
    kernel = w_dilated[0].reshape(9, count, count)
    extended = halo(features, FIRST_DILATION)
    hidden = hidden_of(
        extended, kernel, norm_gain[0, 0], norm_bias[0, 0], FIRST_DILATION, tile_rows, tile_cols
    )
    output_map = block_output(features, hidden, norm_gain[0], norm_bias[0], w_pointwise[0])
    state = mean_of(output_map, mirror_tile(output_map))

    kernel = w_dilated[1]
    both = jnp.concatenate([kernel, jnp.swapaxes(kernel, 0, 1)], axis=2).reshape(9, 2 * count, count)
    extended = halo(state, SECOND_DILATION)
    gain = jnp.concatenate([norm_gain[1, 0], norm_gain[1, 0]])
    bias = jnp.concatenate([norm_bias[1, 0], norm_bias[1, 0]])
    hidden = hidden_of(extended, both, gain, bias, SECOND_DILATION, tile_rows, tile_cols)
    direct = block_output(state, hidden[:count], norm_gain[1], norm_bias[1], w_pointwise[1])
    mirrored = block_output(state, hidden[count:], norm_gain[1], norm_bias[1], w_pointwise[1])
    return mean_of(direct, mirrored)


def solution(mesh):
    in_specs = (P(None, "row", "col"), P(), P(), P(), P())
    out_specs = P(None, "row", "col")
    return jax.shard_map(body, mesh=mesh, in_specs=in_specs, out_specs=out_specs, check_vma=False)
```

```python
import jax
import jax.numpy as jnp
from jax import lax
from jax.sharding import PartitionSpec as P

FIRST_DILATION = 8
SECOND_DILATION = 16


def padded(value, sides, width):
    for axis, dim in sides:
        size, length = (lax.axis_size(axis), value.shape[dim])
        up = [(i, (i + 1) % size) for i in range(size - 1)]
        down = [(j, i) for i, j in up]
        last = lax.slice_in_dim(value, length - width, length, axis=dim)
        initial = lax.slice_in_dim(value, 0, width, axis=dim)
        before = lax.ppermute(last, axis, up)
        after = lax.ppermute(initial, axis, down)
        value = jnp.concatenate([before, value, after], axis=dim)
    return value


def hidden_of(extended_input, kernel, gain, bias, dilation_rate, tile_rows, tile_cols):
    active = jnp.maximum(extended_input, jnp.zeros((), extended_input.dtype))
    windows = [
        lax.slice(
            active,
            (0, p * dilation_rate, q * dilation_rate),
            (active.shape[0], p * dilation_rate + tile_rows, q * dilation_rate + tile_cols),
        )
        for p in range(3)
        for q in range(3)
    ]
    stacked = jnp.stack(windows, axis=0)
    spread = jnp.einsum("toc,tchw->ohw", kernel, stacked, preferred_element_type=jnp.float32)
    hidden = jnp.maximum(spread * gain[:, None, None] + bias[:, None, None], 0.0)
    return hidden.astype(jnp.bfloat16)


def block_output(current_state, hidden, gain_pair, bias_pair, pointwise):
    branch = jnp.einsum("oc,chw->ohw", pointwise, hidden, preferred_element_type=jnp.float32)
    summed = (
        current_state.astype(jnp.float32)
        + branch * gain_pair[1][:, None, None]
        + bias_pair[1][:, None, None]
    )
    return lax.reduce_precision(summed, exponent_bits=8, mantissa_bits=7).astype(jnp.bfloat16)


def mirror_pieces(output_map):
    n_col = lax.axis_size("col")
    channel_count, tile_rows, tile_cols = output_map.shape
    k = tile_cols // tile_rows
    c_lo = channel_count // n_col
    flat = tile_rows * tile_rows
    t = output_map.reshape(n_col, c_lo, tile_rows, k, tile_rows)
    t = jnp.transpose(t, (0, 1, 3, 4, 2)).reshape(n_col, c_lo, k, flat)
    t = lax.all_to_all(t, "col", 0, 0, tiled=True)
    t = jnp.transpose(t, (0, 2, 1, 3)).reshape(n_col * k, c_lo, flat)
    t = lax.all_to_all(t, "row", 0, 0, tiled=True)
    t = t.reshape(n_col, k * c_lo, flat)
    t = lax.all_to_all(t, "col", 0, 0, tiled=True)
    t = t.reshape(n_col, k, c_lo, tile_rows, tile_rows)
    return [t[:, s].reshape(channel_count, tile_rows, tile_rows) for s in range(k)]


def mean_of(a, b):
    return ((a.astype(jnp.float32) + b.astype(jnp.float32)) * 0.5).astype(jnp.bfloat16)


def symmetrized(output_map):
    tile_rows = output_map.shape[1]
    halves = [
        mean_of(output_map[:, :, s * tile_rows:(s + 1) * tile_rows], piece)
        for s, piece in enumerate(mirror_pieces(output_map))
    ]
    return jnp.concatenate(halves, axis=2)


def body(features, w_dilated, w_pointwise, norm_gain, norm_bias):
    count, tile_rows, tile_cols = features.shape
    kernel = w_dilated[0].reshape(9, count, count)
    extended = padded(features, (("row", 1), ("col", 2)), FIRST_DILATION)
    hidden = hidden_of(
        extended, kernel, norm_gain[0, 0], norm_bias[0, 0], FIRST_DILATION, tile_rows, tile_cols
    )
    output_map = block_output(features, hidden, norm_gain[0], norm_bias[0], w_pointwise[0])
    state = symmetrized(output_map)

    kernel = w_dilated[1]
    both = jnp.concatenate([kernel, jnp.swapaxes(kernel, 0, 1)], axis=2).reshape(9, 2 * count, count)
    extended = padded(state, (("row", 1), ("col", 2)), SECOND_DILATION)
    gain = jnp.concatenate([norm_gain[1, 0], norm_gain[1, 0]])
    bias = jnp.concatenate([norm_bias[1, 0], norm_bias[1, 0]])
    hidden = hidden_of(extended, both, gain, bias, SECOND_DILATION, tile_rows, tile_cols)
    direct = block_output(state, hidden[:count], norm_gain[1], norm_bias[1], w_pointwise[1])
    mirrored = block_output(state, hidden[count:], norm_gain[1], norm_bias[1], w_pointwise[1])
    return mean_of(direct, mirrored)


def solution(mesh):
    in_specs = (P(None, "row", "col"), P(), P(), P(), P())
    out_specs = P(None, "row", "col")
    return jax.shard_map(body, mesh=mesh, in_specs=in_specs, out_specs=out_specs, check_vma=False)
```

```python
import jax
import jax.numpy as jnp
from jax import lax
from jax.sharding import PartitionSpec as P

FIRST_DILATION = 8
SECOND_DILATION = 16


def padded(value, sides, width):
    for axis, dim in sides:
        size, length = (lax.axis_size(axis), value.shape[dim])
        up = [(i, (i + 1) % size) for i in range(size - 1)]
        down = [(j, i) for i, j in up]
        last = lax.slice_in_dim(value, length - width, length, axis=dim)
        initial = lax.slice_in_dim(value, 0, width, axis=dim)
        before = lax.ppermute(last, axis, up)
        after = lax.ppermute(initial, axis, down)
        value = jnp.concatenate([before, value, after], axis=dim)
    return value


def hidden_of(extended_input, kernel, gain, bias, dilation_rate, tile_rows, tile_cols):
    active = jnp.maximum(extended_input, jnp.zeros((), extended_input.dtype))
    windows = [
        lax.slice(
            active,
            (0, p * dilation_rate, q * dilation_rate),
            (active.shape[0], p * dilation_rate + tile_rows, q * dilation_rate + tile_cols),
        )
        for p in range(3)
        for q in range(3)
    ]
    stacked = jnp.stack(windows, axis=0)
    spread = jnp.einsum("toc,tchw->ohw", kernel, stacked, preferred_element_type=jnp.float32)
    hidden = jnp.maximum(spread * gain[:, None, None] + bias[:, None, None], 0.0)
    return hidden.astype(jnp.bfloat16)


def block_output(current_state, hidden, gain_pair, bias_pair, pointwise):
    branch = jnp.einsum("oc,chw->ohw", pointwise, hidden, preferred_element_type=jnp.float32)
    summed = (
        current_state.astype(jnp.float32)
        + branch * gain_pair[1][:, None, None]
        + bias_pair[1][:, None, None]
    )
    return lax.reduce_precision(summed, exponent_bits=8, mantissa_bits=7).astype(jnp.bfloat16)


def mirror_pieces(output_map):
    n_col = lax.axis_size("col")
    channel_count, tile_rows, tile_cols = output_map.shape
    k = tile_cols // tile_rows
    c_lo = channel_count // n_col
    lanes = 128
    fold = lanes // tile_rows
    rows = tile_rows // fold
    t = output_map.reshape(n_col, c_lo, tile_rows, k, rows, fold)
    t = jnp.transpose(t, (0, 1, 3, 4, 5, 2)).reshape(n_col, c_lo * k * rows, lanes)
    t = lax.all_to_all(t, "col", 0, 0, tiled=True)
    t = t.reshape(n_col, c_lo, k, rows, lanes)
    t = jnp.transpose(t, (0, 2, 1, 3, 4)).reshape(n_col * k, c_lo * rows, lanes)
    t = lax.all_to_all(t, "row", 0, 0, tiled=True)
    t = t.reshape(n_col, k * c_lo * rows, lanes)
    t = lax.all_to_all(t, "col", 0, 0, tiled=True)
    t = t.reshape(n_col, k, c_lo, rows, fold, tile_rows)
    return [t[:, s].reshape(channel_count, tile_rows, tile_rows) for s in range(k)]


def mean_of(a, b):
    return ((a.astype(jnp.float32) + b.astype(jnp.float32)) * 0.5).astype(jnp.bfloat16)


def symmetrized(output_map):
    tile_rows = output_map.shape[1]
    halves = [
        mean_of(output_map[:, :, s * tile_rows:(s + 1) * tile_rows], piece)
        for s, piece in enumerate(mirror_pieces(output_map))
    ]
    return jnp.concatenate(halves, axis=2)


def body(features, w_dilated, w_pointwise, norm_gain, norm_bias):
    count, tile_rows, tile_cols = features.shape
    kernel = w_dilated[0].reshape(9, count, count)
    extended = padded(features, (("row", 1), ("col", 2)), FIRST_DILATION)
    hidden = hidden_of(
        extended, kernel, norm_gain[0, 0], norm_bias[0, 0], FIRST_DILATION, tile_rows, tile_cols
    )
    output_map = block_output(features, hidden, norm_gain[0], norm_bias[0], w_pointwise[0])
    state = symmetrized(output_map)

    kernel = w_dilated[1]
    both = jnp.concatenate([kernel, jnp.swapaxes(kernel, 0, 1)], axis=2).reshape(9, 2 * count, count)
    extended = padded(state, (("row", 1), ("col", 2)), SECOND_DILATION)
    gain = jnp.concatenate([norm_gain[1, 0], norm_gain[1, 0]])
    bias = jnp.concatenate([norm_bias[1, 0], norm_bias[1, 0]])
    hidden = hidden_of(extended, both, gain, bias, SECOND_DILATION, tile_rows, tile_cols)
    direct = block_output(state, hidden[:count], norm_gain[1], norm_bias[1], w_pointwise[1])
    mirrored = block_output(state, hidden[count:], norm_gain[1], norm_bias[1], w_pointwise[1])
    return mean_of(direct, mirrored)


def solution(mesh):
    in_specs = (P(None, "row", "col"), P(), P(), P(), P())
    out_specs = P(None, "row", "col")
    return jax.shard_map(body, mesh=mesh, in_specs=in_specs, out_specs=out_specs, check_vma=False)
```

```python
import jax
import jax.numpy as jnp
from jax import lax
from jax.sharding import PartitionSpec as P

FIRST_DILATION = 8
SECOND_DILATION = 16


def padded(value, sides):
    for axis, dim, width in sides:
        size, length = (lax.axis_size(axis), value.shape[dim])
        up = [(i, (i + 1) % size) for i in range(size - 1)]
        down = [(j, i) for i, j in up]
        last = lax.slice_in_dim(value, length - width, length, axis=dim)
        initial = lax.slice_in_dim(value, 0, width, axis=dim)
        before = lax.ppermute(last, axis, up)
        after = lax.ppermute(initial, axis, down)
        value = jnp.concatenate([before, value, after], axis=dim)
    return value


def hidden_of(extended_input, kernel, gain, bias, dilation_rate, tile_rows, tile_cols):
    active = jnp.maximum(extended_input, jnp.zeros((), extended_input.dtype))
    windows = [
        lax.slice(
            active,
            (0, p * dilation_rate, q * dilation_rate),
            (active.shape[0], p * dilation_rate + tile_rows, q * dilation_rate + tile_cols),
        )
        for p in range(3)
        for q in range(3)
    ]
    stacked = jnp.stack(windows, axis=0)
    spread = jnp.einsum("toc,tchw->ohw", kernel, stacked, preferred_element_type=jnp.float32)
    hidden = jnp.maximum(spread * gain[:, None, None] + bias[:, None, None], 0.0)
    return hidden.astype(jnp.bfloat16)


def block_output(current_state, hidden, gain_pair, bias_pair, pointwise):
    branch = jnp.einsum("oc,chw->ohw", pointwise, hidden, preferred_element_type=jnp.float32)
    summed = (
        current_state.astype(jnp.float32)
        + branch * gain_pair[1][:, None, None]
        + bias_pair[1][:, None, None]
    )
    return lax.reduce_precision(summed, exponent_bits=8, mantissa_bits=7).astype(jnp.bfloat16)


def mirror_extended(output_map, reach):
    n_col = lax.axis_size("col")
    channel_count, tile_rows, tile_cols = output_map.shape
    k = tile_cols // tile_rows
    c_lo = channel_count // n_col
    lanes = 128
    fold = lanes // tile_rows
    rows = tile_rows // fold
    t = output_map.reshape(n_col, c_lo, rows, fold, k, tile_rows)
    t = jnp.transpose(t, (0, 1, 4, 2, 3, 5)).reshape(n_col, c_lo * k * rows, lanes)
    t = lax.all_to_all(t, "col", 0, 0, tiled=True)
    t = t.reshape(n_col, c_lo, k, rows, lanes)
    t = jnp.transpose(t, (0, 2, 1, 3, 4)).reshape(n_col * k, c_lo * rows, lanes)
    t = lax.all_to_all(t, "row", 0, 0, tiled=True)
    n_row = n_col * k
    t = t.reshape(n_row, c_lo, rows, lanes)
    t = jnp.transpose(t, (1, 0, 2, 3)).reshape(c_lo, n_row * rows, lanes)
    edge = reach // fold
    step = tile_cols // fold
    span = step + 2 * edge
    t = jnp.pad(t, ((0, 0), (edge, edge), (0, 0)))
    t = jnp.stack([t[:, z * step:z * step + span] for z in range(n_col)])
    t = lax.all_to_all(t.reshape(n_col, c_lo * span, lanes), "col", 0, 0, tiled=True)
    t = t.reshape(channel_count, span, fold, tile_rows)
    return jnp.transpose(t, (0, 3, 1, 2)).reshape(channel_count, tile_rows, span * fold)


def mean_of(a, b):
    return ((a.astype(jnp.float32) + b.astype(jnp.float32)) * 0.5).astype(jnp.bfloat16)


def body(features, w_dilated, w_pointwise, norm_gain, norm_bias):
    count, tile_rows, tile_cols = features.shape
    reach = SECOND_DILATION

    kernel = w_dilated[0].reshape(9, count, count)
    extended = padded(features, (("row", 1, FIRST_DILATION), ("col", 2, FIRST_DILATION + reach)))
    wide = tile_cols + 2 * reach
    hidden = hidden_of(
        extended, kernel, norm_gain[0, 0], norm_bias[0, 0], FIRST_DILATION, tile_rows, wide
    )
    own = extended[:, FIRST_DILATION:FIRST_DILATION + tile_rows, FIRST_DILATION:FIRST_DILATION + wide]
    output_map = block_output(own, hidden, norm_gain[0], norm_bias[0], w_pointwise[0])
    mirrored = mirror_extended(output_map[:, :, reach:reach + tile_cols], reach)
    first = lax.axis_index("col") * tile_cols - reach
    columns = first + lax.broadcasted_iota(jnp.int32, (1, 1, wide), 2)
    inside = (columns >= 0) & (columns < lax.axis_size("col") * tile_cols)
    state = jnp.where(inside, mean_of(output_map, mirrored), jnp.zeros((), jnp.bfloat16))

    kernel = w_dilated[1]
    both = jnp.concatenate([kernel, jnp.swapaxes(kernel, 0, 1)], axis=2).reshape(9, 2 * count, count)
    extended = padded(state, (("row", 1, SECOND_DILATION),))
    gain = jnp.concatenate([norm_gain[1, 0], norm_gain[1, 0]])
    bias = jnp.concatenate([norm_bias[1, 0], norm_bias[1, 0]])
    hidden = hidden_of(extended, both, gain, bias, SECOND_DILATION, tile_rows, tile_cols)
    own = state[:, :, reach:reach + tile_cols]
    direct = block_output(own, hidden[:count], norm_gain[1], norm_bias[1], w_pointwise[1])
    mirrored = block_output(own, hidden[count:], norm_gain[1], norm_bias[1], w_pointwise[1])
    return mean_of(direct, mirrored)


def solution(mesh):
    in_specs = (P(None, "row", "col"), P(), P(), P(), P())
    out_specs = P(None, "row", "col")
    return jax.shard_map(body, mesh=mesh, in_specs=in_specs, out_specs=out_specs, check_vma=False)
```

```python
import jax
import jax.numpy as jnp
from jax import lax
from jax.sharding import PartitionSpec as P

FIRST_DILATION = 8
SECOND_DILATION = 16


def padded(value, sides, width):
    for axis, dim in sides:
        size, length = (lax.axis_size(axis), value.shape[dim])
        up = [(i, (i + 1) % size) for i in range(size - 1)]
        down = [(j, i) for i, j in up]
        last = lax.slice_in_dim(value, length - width, length, axis=dim)
        initial = lax.slice_in_dim(value, 0, width, axis=dim)
        before = lax.ppermute(last, axis, up)
        after = lax.ppermute(initial, axis, down)
        value = jnp.concatenate([before, value, after], axis=dim)
    return value


def hidden_of(extended_input, kernel, gain, bias, dilation_rate, tile_rows, tile_cols):
    active = jnp.maximum(extended_input, jnp.zeros((), extended_input.dtype))
    windows = [
        lax.slice(
            active,
            (0, p * dilation_rate, q * dilation_rate),
            (active.shape[0], p * dilation_rate + tile_rows, q * dilation_rate + tile_cols),
        )
        for p in range(3)
        for q in range(3)
    ]
    stacked = jnp.stack(windows, axis=0)
    spread = jnp.einsum("toc,tchw->ohw", kernel, stacked, preferred_element_type=jnp.float32)
    hidden = jnp.maximum(spread * gain[:, None, None] + bias[:, None, None], 0.0)
    return hidden.astype(jnp.bfloat16)


def block_output(current_state, hidden, gain_pair, bias_pair, pointwise):
    branch = jnp.einsum("oc,chw->ohw", pointwise, hidden, preferred_element_type=jnp.float32)
    summed = (
        current_state.astype(jnp.float32)
        + branch * gain_pair[1][:, None, None]
        + bias_pair[1][:, None, None]
    )
    return lax.reduce_precision(summed, exponent_bits=8, mantissa_bits=7).astype(jnp.bfloat16)


def mirror_pieces(output_map):
    n_col = lax.axis_size("col")
    channel_count, tile_rows, tile_cols = output_map.shape
    k = tile_cols // tile_rows
    c_lo = channel_count // n_col
    lanes = 128
    fold = lanes // tile_rows
    rows = tile_rows // fold
    t = output_map.reshape(n_col, c_lo, tile_rows, k, rows, fold)
    t = jnp.transpose(t, (0, 1, 3, 4, 5, 2)).reshape(n_col, c_lo * k * rows, lanes)
    t = lax.all_to_all(t, "col", 0, 0, tiled=True)
    t = t.reshape(n_col, c_lo, k, rows, lanes)
    t = jnp.transpose(t, (0, 2, 1, 3, 4)).reshape(n_col * k, c_lo * rows, lanes)
    t = lax.all_to_all(t, "row", 0, 0, tiled=True)
    t = t.reshape(n_col, k * c_lo * rows, lanes)
    t = lax.all_to_all(t, "col", 0, 0, tiled=True)
    t = t.reshape(n_col, k, c_lo, rows, fold, tile_rows)
    return [t[:, s].reshape(channel_count, tile_rows, tile_rows) for s in range(k)]


def mean_of(a, b):
    return ((a.astype(jnp.float32) + b.astype(jnp.float32)) * 0.5).astype(jnp.bfloat16)


def symmetrized(output_map):
    tile_rows = output_map.shape[1]
    halves = [
        mean_of(output_map[:, :, s * tile_rows:(s + 1) * tile_rows], piece)
        for s, piece in enumerate(mirror_pieces(output_map))
    ]
    return jnp.concatenate(halves, axis=2)


def body(features, w_dilated, w_pointwise, norm_gain, norm_bias):
    count, tile_rows, tile_cols = features.shape
    kernel = w_dilated[0].reshape(9, count, count)
    extended = padded(features, (("col", 2), ("row", 1)), FIRST_DILATION)
    hidden = hidden_of(
        extended, kernel, norm_gain[0, 0], norm_bias[0, 0], FIRST_DILATION, tile_rows, tile_cols
    )
    output_map = block_output(features, hidden, norm_gain[0], norm_bias[0], w_pointwise[0])
    state = symmetrized(output_map)

    kernel = w_dilated[1]
    both = jnp.concatenate([kernel, jnp.swapaxes(kernel, 0, 1)], axis=2).reshape(9, 2 * count, count)
    extended = padded(state, (("col", 2), ("row", 1)), SECOND_DILATION)
    gain = jnp.concatenate([norm_gain[1, 0], norm_gain[1, 0]])
    bias = jnp.concatenate([norm_bias[1, 0], norm_bias[1, 0]])
    hidden = hidden_of(extended, both, gain, bias, SECOND_DILATION, tile_rows, tile_cols)
    direct = block_output(state, hidden[:count], norm_gain[1], norm_bias[1], w_pointwise[1])
    mirrored = block_output(state, hidden[count:], norm_gain[1], norm_bias[1], w_pointwise[1])
    return mean_of(direct, mirrored)


def solution(mesh):
    in_specs = (P(None, "row", "col"), P(), P(), P(), P())
    out_specs = P(None, "row", "col")
    return jax.shard_map(body, mesh=mesh, in_specs=in_specs, out_specs=out_specs, check_vma=False)
```

```python
import jax
import jax.numpy as jnp
from jax import lax
from jax.sharding import PartitionSpec as P

FIRST_DILATION = 8
SECOND_DILATION = 16


def padded(value, sides, width):
    for axis, dim in sides:
        size, length = (lax.axis_size(axis), value.shape[dim])
        up = [(i, (i + 1) % size) for i in range(size - 1)]
        down = [(j, i) for i, j in up]
        last = lax.slice_in_dim(value, length - width, length, axis=dim)
        initial = lax.slice_in_dim(value, 0, width, axis=dim)
        before = lax.ppermute(last, axis, up)
        after = lax.ppermute(initial, axis, down)
        value = jnp.concatenate([before, value, after], axis=dim)
    return value


def hidden_of(extended_input, kernel, gain, bias, dilation_rate, tile_rows, tile_cols):
    active = jnp.maximum(extended_input, jnp.zeros((), extended_input.dtype))
    windows = [
        lax.slice(
            active,
            (0, p * dilation_rate, q * dilation_rate),
            (active.shape[0], p * dilation_rate + tile_rows, q * dilation_rate + tile_cols),
        )
        for p in range(3)
        for q in range(3)
    ]
    stacked = jnp.stack(windows, axis=0)
    spread = jnp.einsum("toc,tchw->ohw", kernel, stacked, preferred_element_type=jnp.float32)
    hidden = jnp.maximum(spread * gain[:, None, None] + bias[:, None, None], 0.0)
    return hidden.astype(jnp.bfloat16)


def block_output(current_state, hidden, gain_pair, bias_pair, pointwise):
    branch = jnp.einsum("oc,chw->ohw", pointwise, hidden, preferred_element_type=jnp.float32)
    summed = (
        current_state.astype(jnp.float32)
        + branch * gain_pair[1][:, None, None]
        + bias_pair[1][:, None, None]
    )
    return lax.reduce_precision(summed, exponent_bits=8, mantissa_bits=7).astype(jnp.bfloat16)


def mirror_pieces(output_map):
    n_col = lax.axis_size("col")
    channel_count, tile_rows, tile_cols = output_map.shape
    k = tile_cols // tile_rows
    c_lo = channel_count // n_col
    lanes = 128
    fold = lanes // tile_rows
    rows = tile_rows // fold
    t = output_map.reshape(n_col, c_lo, tile_rows, k, rows, fold)
    t = jnp.transpose(t, (0, 1, 3, 4, 5, 2)).reshape(n_col, c_lo * k * rows, lanes)
    t = lax.all_to_all(t, "col", 0, 0, tiled=True)
    t = t.reshape(n_col, c_lo, k, rows, lanes)
    t = jnp.transpose(t, (0, 2, 1, 3, 4)).reshape(n_col * k, c_lo * rows, lanes)
    t = lax.all_to_all(t, "row", 0, 0, tiled=True)
    t = t.reshape(n_col, k * c_lo * rows, lanes)
    t = lax.all_to_all(t, "col", 0, 0, tiled=True)
    t = t.reshape(n_col, k, c_lo, rows, fold, tile_rows)
    return [t[:, s].reshape(channel_count, tile_rows, tile_rows) for s in range(k)]


def mean_of(a, b):
    return ((a.astype(jnp.float32) + b.astype(jnp.float32)) * 0.5).astype(jnp.bfloat16)


def symmetrized(output_map):
    tile_rows = output_map.shape[1]
    halves = [
        mean_of(output_map[:, :, s * tile_rows:(s + 1) * tile_rows], piece)
        for s, piece in enumerate(mirror_pieces(output_map))
    ]
    return jnp.concatenate(halves, axis=2)


def body(features, w_dilated, w_pointwise, norm_gain, norm_bias):
    count, tile_rows, tile_cols = features.shape
    kernel = w_dilated[0].reshape(9, count, count)
    extended = padded(features, (("row", 1), ("col", 2)), FIRST_DILATION)
    hidden = hidden_of(
        extended, kernel, norm_gain[0, 0], norm_bias[0, 0], FIRST_DILATION, tile_rows, tile_cols
    )
    hidden = lax.optimization_barrier(hidden)
    output_map = block_output(features, hidden, norm_gain[0], norm_bias[0], w_pointwise[0])
    state = symmetrized(output_map)

    kernel = w_dilated[1]
    both = jnp.concatenate([kernel, jnp.swapaxes(kernel, 0, 1)], axis=2).reshape(9, 2 * count, count)
    extended = padded(state, (("row", 1), ("col", 2)), SECOND_DILATION)
    gain = jnp.concatenate([norm_gain[1, 0], norm_gain[1, 0]])
    bias = jnp.concatenate([norm_bias[1, 0], norm_bias[1, 0]])
    hidden = hidden_of(extended, both, gain, bias, SECOND_DILATION, tile_rows, tile_cols)
    direct = block_output(state, hidden[:count], norm_gain[1], norm_bias[1], w_pointwise[1])
    mirrored = block_output(state, hidden[count:], norm_gain[1], norm_bias[1], w_pointwise[1])
    return mean_of(direct, mirrored)


def solution(mesh):
    in_specs = (P(None, "row", "col"), P(), P(), P(), P())
    out_specs = P(None, "row", "col")
    return jax.shard_map(body, mesh=mesh, in_specs=in_specs, out_specs=out_specs, check_vma=False)
```

```python
import jax
import jax.numpy as jnp
from jax import lax
from jax.sharding import PartitionSpec as P

FIRST_DILATION = 8
SECOND_DILATION = 16


def padded(value, sides, width):
    for axis, dim in sides:
        size, length = (lax.axis_size(axis), value.shape[dim])
        up = [(i, (i + 1) % size) for i in range(size - 1)]
        down = [(j, i) for i, j in up]
        last = lax.slice_in_dim(value, length - width, length, axis=dim)
        initial = lax.slice_in_dim(value, 0, width, axis=dim)
        before = lax.ppermute(last, axis, up)
        after = lax.ppermute(initial, axis, down)
        value = jnp.concatenate([before, value, after], axis=dim)
    return value


def hidden_of(extended_input, kernel, gain, bias, dilation_rate, tile_rows, tile_cols):
    active = jnp.maximum(extended_input, jnp.zeros((), extended_input.dtype))
    windows = [
        lax.slice(
            active,
            (0, p * dilation_rate, q * dilation_rate),
            (active.shape[0], p * dilation_rate + tile_rows, q * dilation_rate + tile_cols),
        )
        for p in range(3)
        for q in range(3)
    ]
    stacked = jnp.stack(windows, axis=0)
    spread = jnp.einsum("toc,tchw->ohw", kernel, stacked, preferred_element_type=jnp.float32)
    hidden = jnp.maximum(spread * gain[:, None, None] + bias[:, None, None], 0.0)
    return hidden.astype(jnp.bfloat16)


def block_output(current_state, hidden, gain_pair, bias_pair, pointwise):
    branch = jnp.einsum("oc,chw->ohw", pointwise, hidden, preferred_element_type=jnp.float32)
    summed = (
        current_state.astype(jnp.float32)
        + branch * gain_pair[1][:, None, None]
        + bias_pair[1][:, None, None]
    )
    return lax.reduce_precision(summed, exponent_bits=8, mantissa_bits=7).astype(jnp.bfloat16)


def mirror_pieces(output_map):
    n_col = lax.axis_size("col")
    channel_count, tile_rows, tile_cols = output_map.shape
    k = tile_cols // tile_rows
    c_lo = channel_count // n_col
    lanes = 128
    fold = lanes // tile_rows
    rows = tile_rows // fold
    t = output_map.reshape(n_col, c_lo, tile_rows, k, rows, fold)
    t = jnp.transpose(t, (0, 1, 3, 4, 5, 2)).reshape(n_col, c_lo * k * rows, lanes)
    t = lax.all_to_all(t, "col", 0, 0, tiled=True)
    t = t.reshape(n_col, c_lo, k, rows, lanes)
    t = jnp.transpose(t, (0, 2, 1, 3, 4)).reshape(n_col * k, c_lo * rows, lanes)
    t = lax.all_to_all(t, "row", 0, 0, tiled=True)
    t = t.reshape(n_col, k * c_lo * rows, lanes)
    t = lax.all_to_all(t, "col", 0, 0, tiled=True)
    t = t.reshape(n_col, k, c_lo, rows, fold, tile_rows)
    t = jnp.transpose(t, (0, 2, 3, 4, 1, 5))
    return t.reshape(channel_count, tile_rows, tile_cols)


def mean_of(a, b):
    return ((a.astype(jnp.float32) + b.astype(jnp.float32)) * 0.5).astype(jnp.bfloat16)


def symmetrized(output_map):
    return mean_of(output_map, lax.optimization_barrier(mirror_pieces(output_map)))


def body(features, w_dilated, w_pointwise, norm_gain, norm_bias):
    count, tile_rows, tile_cols = features.shape
    kernel = w_dilated[0].reshape(9, count, count)
    extended = padded(features, (("row", 1), ("col", 2)), FIRST_DILATION)
    hidden = hidden_of(
        extended, kernel, norm_gain[0, 0], norm_bias[0, 0], FIRST_DILATION, tile_rows, tile_cols
    )
    hidden = lax.optimization_barrier(hidden)
    output_map = block_output(features, hidden, norm_gain[0], norm_bias[0], w_pointwise[0])
    state = symmetrized(output_map)

    kernel = w_dilated[1]
    both = jnp.concatenate([kernel, jnp.swapaxes(kernel, 0, 1)], axis=2).reshape(9, 2 * count, count)
    extended = padded(state, (("row", 1), ("col", 2)), SECOND_DILATION)
    gain = jnp.concatenate([norm_gain[1, 0], norm_gain[1, 0]])
    bias = jnp.concatenate([norm_bias[1, 0], norm_bias[1, 0]])
    hidden = hidden_of(extended, both, gain, bias, SECOND_DILATION, tile_rows, tile_cols)
    direct = block_output(state, hidden[:count], norm_gain[1], norm_bias[1], w_pointwise[1])
    mirrored = block_output(state, hidden[count:], norm_gain[1], norm_bias[1], w_pointwise[1])
    return mean_of(direct, mirrored)


def solution(mesh):
    in_specs = (P(None, "row", "col"), P(), P(), P(), P())
    out_specs = P(None, "row", "col")
    return jax.shard_map(body, mesh=mesh, in_specs=in_specs, out_specs=out_specs, check_vma=False)
```

```python
import jax
import jax.numpy as jnp
from jax import lax
from jax.sharding import PartitionSpec as P

FIRST_DILATION = 8
SECOND_DILATION = 16


def padded(value, sides, width):
    for axis, dim in sides:
        size, length = (lax.axis_size(axis), value.shape[dim])
        up = [(i, (i + 1) % size) for i in range(size - 1)]
        down = [(j, i) for i, j in up]
        last = lax.slice_in_dim(value, length - width, length, axis=dim)
        initial = lax.slice_in_dim(value, 0, width, axis=dim)
        before = lax.ppermute(last, axis, up)
        after = lax.ppermute(initial, axis, down)
        value = jnp.concatenate([before, value, after], axis=dim)
    return value


def hidden_of(extended_input, kernel, gain, bias, dilation_rate, tile_rows, tile_cols):
    active = jnp.maximum(extended_input, jnp.zeros((), extended_input.dtype))
    windows = [
        lax.slice(
            active,
            (0, p * dilation_rate, q * dilation_rate),
            (active.shape[0], p * dilation_rate + tile_rows, q * dilation_rate + tile_cols),
        )
        for p in range(3)
        for q in range(3)
    ]
    stacked = jnp.stack(windows, axis=0)
    spread = jnp.einsum("toc,tchw->ohw", kernel, stacked, preferred_element_type=jnp.float32)
    hidden = jnp.maximum(spread * gain[:, None, None] + bias[:, None, None], 0.0)
    return hidden.astype(jnp.bfloat16)


def block_output(current_state, hidden, gain_pair, bias_pair, pointwise):
    branch = jnp.einsum("oc,chw->ohw", pointwise, hidden, preferred_element_type=jnp.float32)
    summed = (
        current_state.astype(jnp.float32)
        + branch * gain_pair[1][:, None, None]
        + bias_pair[1][:, None, None]
    )
    return lax.reduce_precision(summed, exponent_bits=8, mantissa_bits=7).astype(jnp.bfloat16)


def mirror_pieces(output_map):
    n_col = lax.axis_size("col")
    channel_count, tile_rows, tile_cols = output_map.shape
    k = tile_cols // tile_rows
    c_lo = channel_count // n_col
    lanes = 128
    fold = lanes // tile_rows
    rows = tile_rows // fold
    t = output_map.reshape(n_col, c_lo, tile_rows, k, rows, fold)
    t = jnp.transpose(t, (0, 1, 3, 4, 5, 2)).reshape(n_col, c_lo * k * rows, lanes)
    t = lax.all_to_all(t, "col", 0, 0, tiled=True)
    t = t.reshape(n_col, c_lo, k, rows, lanes)
    t = jnp.transpose(t, (0, 2, 1, 3, 4)).reshape(n_col * k, c_lo * rows, lanes)
    t = lax.all_to_all(t, "row", 0, 0, tiled=True)
    t = t.reshape(n_col, k * c_lo * rows, lanes)
    t = lax.all_to_all(t, "col", 0, 0, tiled=True)
    t = t.reshape(n_col, k, c_lo, rows, fold, tile_rows)
    t = jnp.transpose(t, (0, 2, 3, 4, 1, 5))
    return t.reshape(channel_count, tile_rows, tile_cols)


def mean_of(a, b):
    return ((a.astype(jnp.float32) + b.astype(jnp.float32)) * 0.5).astype(jnp.bfloat16)


def symmetrized(output_map):
    return mean_of(output_map, lax.optimization_barrier(mirror_pieces(output_map)))


def body(features, w_dilated, w_pointwise, norm_gain, norm_bias):
    count, tile_rows, tile_cols = features.shape
    kernel = w_dilated[0].reshape(9, count, count)
    extended = padded(features, (("row", 1), ("col", 2)), FIRST_DILATION)
    hidden = hidden_of(
        extended, kernel, norm_gain[0, 0], norm_bias[0, 0], FIRST_DILATION, tile_rows, tile_cols
    )
    kernel = w_dilated[1]
    both = jnp.concatenate([kernel, jnp.swapaxes(kernel, 0, 1)], axis=2).reshape(9, 2 * count, count)
    gain = jnp.concatenate([norm_gain[1, 0], norm_gain[1, 0]])
    bias = jnp.concatenate([norm_bias[1, 0], norm_bias[1, 0]])
    hidden, both, gain, bias = lax.optimization_barrier((hidden, both, gain, bias))
    output_map = block_output(features, hidden, norm_gain[0], norm_bias[0], w_pointwise[0])
    state = symmetrized(output_map)

    extended = padded(state, (("row", 1), ("col", 2)), SECOND_DILATION)
    hidden = hidden_of(extended, both, gain, bias, SECOND_DILATION, tile_rows, tile_cols)
    direct = block_output(state, hidden[:count], norm_gain[1], norm_bias[1], w_pointwise[1])
    mirrored = block_output(state, hidden[count:], norm_gain[1], norm_bias[1], w_pointwise[1])
    return mean_of(direct, mirrored)


def solution(mesh):
    in_specs = (P(None, "row", "col"), P(), P(), P(), P())
    out_specs = P(None, "row", "col")
    return jax.shard_map(body, mesh=mesh, in_specs=in_specs, out_specs=out_specs, check_vma=False)
```

```python
import jax
import jax.numpy as jnp
from jax import lax
from jax.experimental.layout import Layout, with_layout_constraint
from jax.sharding import PartitionSpec as P

FIRST_DILATION = 8
SECOND_DILATION = 16


def padded(value, sides, width):
    for axis, dim in sides:
        size, length = (lax.axis_size(axis), value.shape[dim])
        up = [(i, (i + 1) % size) for i in range(size - 1)]
        down = [(j, i) for i, j in up]
        last = lax.slice_in_dim(value, length - width, length, axis=dim)
        initial = lax.slice_in_dim(value, 0, width, axis=dim)
        before = lax.ppermute(last, axis, up)
        after = lax.ppermute(initial, axis, down)
        value = jnp.concatenate([before, value, after], axis=dim)
    return value


def hidden_of(extended_input, kernel, gain, bias, dilation_rate, tile_rows, tile_cols):
    active = jnp.maximum(extended_input, jnp.zeros((), extended_input.dtype))
    windows = [
        lax.slice(
            active,
            (0, p * dilation_rate, q * dilation_rate),
            (active.shape[0], p * dilation_rate + tile_rows, q * dilation_rate + tile_cols),
        )
        for p in range(3)
        for q in range(3)
    ]
    stacked = jnp.stack(windows, axis=0)
    spread = jnp.einsum("toc,tchw->ohw", kernel, stacked, preferred_element_type=jnp.float32)
    hidden = jnp.maximum(spread * gain[:, None, None] + bias[:, None, None], 0.0)
    return hidden.astype(jnp.bfloat16)


def block_output(current_state, hidden, gain_pair, bias_pair, pointwise):
    branch = jnp.einsum("oc,chw->ohw", pointwise, hidden, preferred_element_type=jnp.float32)
    summed = (
        current_state.astype(jnp.float32)
        + branch * gain_pair[1][:, None, None]
        + bias_pair[1][:, None, None]
    )
    return lax.reduce_precision(summed, exponent_bits=8, mantissa_bits=7).astype(jnp.bfloat16)


def mirror_pieces(output_map):
    n_col = lax.axis_size("col")
    channel_count, tile_rows, tile_cols = output_map.shape
    k = tile_cols // tile_rows
    c_lo = channel_count // n_col
    lanes = 128
    fold = lanes // tile_rows
    rows = tile_rows // fold
    t = output_map.reshape(n_col, c_lo, tile_rows, k, rows, fold)
    t = jnp.transpose(t, (0, 1, 3, 4, 5, 2)).reshape(n_col, c_lo * k * rows, lanes)
    t = lax.all_to_all(t, "col", 0, 0, tiled=True)
    t = t.reshape(n_col, c_lo, k, rows, lanes)
    t = jnp.transpose(t, (0, 2, 1, 3, 4)).reshape(n_col * k, c_lo * rows, lanes)
    t = lax.all_to_all(t, "row", 0, 0, tiled=True)
    t = t.reshape(n_col, k * c_lo * rows, lanes)
    t = lax.all_to_all(t, "col", 0, 0, tiled=True)
    t = t.reshape(n_col, k, c_lo, rows, fold, tile_rows)
    t = jnp.transpose(t, (0, 2, 3, 4, 1, 5))
    return t.reshape(channel_count, tile_rows, tile_cols)


def mean_of(a, b):
    return ((a.astype(jnp.float32) + b.astype(jnp.float32)) * 0.5).astype(jnp.bfloat16)


def symmetrized(output_map):
    return mean_of(output_map, lax.optimization_barrier(mirror_pieces(output_map)))


def body(features, w_dilated, w_pointwise, norm_gain, norm_bias):
    count, tile_rows, tile_cols = features.shape
    kernel = w_dilated[0].reshape(9, count, count)
    extended = padded(features, (("row", 1), ("col", 2)), FIRST_DILATION)
    hidden = hidden_of(
        extended, kernel, norm_gain[0, 0], norm_bias[0, 0], FIRST_DILATION, tile_rows, tile_cols
    )
    hidden = lax.optimization_barrier(hidden)
    output_map = block_output(features, hidden, norm_gain[0], norm_bias[0], w_pointwise[0])
    state = symmetrized(output_map)

    kernel = w_dilated[1]
    both = jnp.concatenate([kernel, jnp.swapaxes(kernel, 0, 1)], axis=2).reshape(9, 2 * count, count)
    extended = padded(state, (("row", 1), ("col", 2)), SECOND_DILATION)
    gain = jnp.concatenate([norm_gain[1, 0], norm_gain[1, 0]])
    bias = jnp.concatenate([norm_bias[1, 0], norm_bias[1, 0]])
    hidden = hidden_of(extended, both, gain, bias, SECOND_DILATION, tile_rows, tile_cols)
    direct = block_output(state, hidden[:count], norm_gain[1], norm_bias[1], w_pointwise[1])
    mirrored = block_output(state, hidden[count:], norm_gain[1], norm_bias[1], w_pointwise[1])
    return with_layout_constraint(mean_of(direct, mirrored), Layout(major_to_minor=(0, 1, 2)))


def solution(mesh):
    in_specs = (P(None, "row", "col"), P(), P(), P(), P())
    out_specs = P(None, "row", "col")
    return jax.shard_map(body, mesh=mesh, in_specs=in_specs, out_specs=out_specs, check_vma=False)
```

```python
import jax
import jax.numpy as jnp
from jax import lax
from jax.sharding import PartitionSpec as P

FIRST_DILATION = 8
SECOND_DILATION = 16


def padded(value, sides, width):
    for axis, dim in sides:
        size, length = (lax.axis_size(axis), value.shape[dim])
        up = [(i, (i + 1) % size) for i in range(size - 1)]
        down = [(j, i) for i, j in up]
        last = lax.slice_in_dim(value, length - width, length, axis=dim)
        initial = lax.slice_in_dim(value, 0, width, axis=dim)
        before = lax.ppermute(last, axis, up)
        after = lax.ppermute(initial, axis, down)
        value = jnp.concatenate([before, value, after], axis=dim)
    return value


def hidden_of(extended_input, kernel, gain, bias, dilation_rate, tile_rows, tile_cols):
    active = jnp.maximum(extended_input, jnp.zeros((), extended_input.dtype))
    windows = [
        lax.slice(
            active,
            (0, p * dilation_rate, q * dilation_rate),
            (active.shape[0], p * dilation_rate + tile_rows, q * dilation_rate + tile_cols),
        )
        for p in range(3)
        for q in range(3)
    ]
    stacked = jnp.stack(windows, axis=0)
    spread = jnp.einsum("toc,tchw->ohw", kernel, stacked, preferred_element_type=jnp.float32)
    hidden = jnp.maximum(spread * gain[:, None, None] + bias[:, None, None], 0.0)
    return hidden.astype(jnp.bfloat16)


def block_output(current_state, hidden, gain_pair, bias_pair, pointwise):
    branch = jnp.einsum("oc,chw->ohw", pointwise, hidden, preferred_element_type=jnp.float32)
    summed = (
        current_state.astype(jnp.float32)
        + branch * gain_pair[1][:, None, None]
        + bias_pair[1][:, None, None]
    )
    return lax.reduce_precision(summed, exponent_bits=8, mantissa_bits=7).astype(jnp.bfloat16)


def mirror_pieces(output_map):
    n_col = lax.axis_size("col")
    channel_count, tile_rows, tile_cols = output_map.shape
    k = tile_cols // tile_rows
    c_lo = channel_count // n_col
    lanes = 128
    fold = lanes // tile_rows
    rows = tile_rows // fold
    t = output_map.reshape(n_col, c_lo, tile_rows, k, rows, fold)
    t = jnp.transpose(t, (0, 1, 3, 4, 5, 2)).reshape(n_col, c_lo * k * rows, lanes)
    t = lax.all_to_all(t, "col", 0, 0, tiled=True)
    t = t.reshape(n_col, c_lo, k, rows, lanes)
    t = jnp.transpose(t, (0, 2, 1, 3, 4)).reshape(n_col * k, c_lo * rows, lanes)
    t = lax.all_to_all(t, "row", 0, 0, tiled=True)
    t = t.reshape(n_col, k * c_lo * rows, lanes)
    t = lax.all_to_all(t, "col", 0, 0, tiled=True)
    t = t.reshape(n_col, k, c_lo, rows, fold, tile_rows)
    t = jnp.transpose(t, (0, 2, 3, 4, 1, 5))
    return t.reshape(channel_count, tile_rows, tile_cols)


def mean_of(a, b):
    return ((a.astype(jnp.float32) + b.astype(jnp.float32)) * 0.5).astype(jnp.bfloat16)


def symmetrized(output_map):
    return mean_of(output_map, lax.optimization_barrier(mirror_pieces(output_map)))


def body(features, w_dilated, w_pointwise, norm_gain, norm_bias):
    count, tile_rows, tile_cols = features.shape
    kernel = w_dilated[0].reshape(9, count, count)
    extended = padded(features, (("row", 1), ("col", 2)), FIRST_DILATION)
    hidden = hidden_of(
        extended, kernel, norm_gain[0, 0], norm_bias[0, 0], FIRST_DILATION, tile_rows, tile_cols
    )
    hidden = lax.optimization_barrier(hidden)
    output_map = block_output(features, hidden, norm_gain[0], norm_bias[0], w_pointwise[0])
    state = symmetrized(output_map)

    kernel = w_dilated[1]
    both = jnp.concatenate([kernel, jnp.swapaxes(kernel, 0, 1)], axis=2).reshape(9, 2 * count, count)
    extended = padded(state, (("col", 2), ("row", 1)), SECOND_DILATION)
    gain = jnp.concatenate([norm_gain[1, 0], norm_gain[1, 0]])
    bias = jnp.concatenate([norm_bias[1, 0], norm_bias[1, 0]])
    hidden = hidden_of(extended, both, gain, bias, SECOND_DILATION, tile_rows, tile_cols)
    direct = block_output(state, hidden[:count], norm_gain[1], norm_bias[1], w_pointwise[1])
    mirrored = block_output(state, hidden[count:], norm_gain[1], norm_bias[1], w_pointwise[1])
    return mean_of(direct, mirrored)


def solution(mesh):
    in_specs = (P(None, "row", "col"), P(), P(), P(), P())
    out_specs = P(None, "row", "col")
    return jax.shard_map(body, mesh=mesh, in_specs=in_specs, out_specs=out_specs, check_vma=False)
```

```python
import jax
import jax.numpy as jnp
from jax import lax
from jax.sharding import PartitionSpec as P

FIRST_DILATION = 8
SECOND_DILATION = 16


def padded(value, sides, width):
    for axis, dim in sides:
        size, length = (lax.axis_size(axis), value.shape[dim])
        up = [(i, (i + 1) % size) for i in range(size - 1)]
        down = [(j, i) for i, j in up]
        last = lax.slice_in_dim(value, length - width, length, axis=dim)
        initial = lax.slice_in_dim(value, 0, width, axis=dim)
        before = lax.ppermute(last, axis, up)
        after = lax.ppermute(initial, axis, down)
        value = jnp.concatenate([before, value, after], axis=dim)
    return value


def hidden_of(extended_input, kernel, gain, bias, dilation_rate, tile_rows, tile_cols):
    active = jnp.maximum(extended_input, jnp.zeros((), extended_input.dtype))
    windows = [
        lax.slice(
            active,
            (0, p * dilation_rate, q * dilation_rate),
            (active.shape[0], p * dilation_rate + tile_rows, q * dilation_rate + tile_cols),
        )
        for p in range(3)
        for q in range(3)
    ]
    stacked = jnp.stack(windows, axis=0)
    spread = jnp.einsum("toc,tchw->ohw", kernel, stacked, preferred_element_type=jnp.float32)
    hidden = jnp.maximum(spread * gain[:, None, None] + bias[:, None, None], 0.0)
    return hidden.astype(jnp.bfloat16)


def block_output(current_state, hidden, gain_pair, bias_pair, pointwise):
    branch = jnp.einsum("oc,chw->ohw", pointwise, hidden, preferred_element_type=jnp.float32)
    summed = (
        current_state.astype(jnp.float32)
        + branch * gain_pair[1][:, None, None]
        + bias_pair[1][:, None, None]
    )
    return lax.reduce_precision(summed, exponent_bits=8, mantissa_bits=7).astype(jnp.bfloat16)


def mirror_pieces(output_map):
    n_col = lax.axis_size("col")
    channel_count, tile_rows, tile_cols = output_map.shape
    k = tile_cols // tile_rows
    c_lo = channel_count // n_col
    lanes = 128
    fold = lanes // tile_rows
    rows = tile_rows // fold
    t = output_map.reshape(n_col, c_lo, tile_rows, k, rows, fold)
    t = jnp.transpose(t, (0, 1, 3, 4, 5, 2)).reshape(n_col, c_lo * k * rows, lanes)
    t = lax.all_to_all(t, "col", 0, 0, tiled=True)
    t = t.reshape(n_col, c_lo, k, rows, lanes)
    t = jnp.transpose(t, (0, 2, 1, 3, 4)).reshape(n_col * k, c_lo * rows, lanes)
    t = lax.all_to_all(t, "row", 0, 0, tiled=True)
    t = t.reshape(n_col, k * c_lo * rows, lanes)
    t = lax.all_to_all(t, "col", 0, 0, tiled=True)
    t = t.reshape(n_col, k, c_lo, rows, fold, tile_rows)
    t = jnp.transpose(t, (0, 2, 3, 4, 1, 5))
    return t.reshape(channel_count, tile_rows, tile_cols)


def mean_of(a, b):
    return ((a.astype(jnp.float32) + b.astype(jnp.float32)) * 0.5).astype(jnp.bfloat16)


def symmetrized(output_map, width):
    mirrored = lax.optimization_barrier(mirror_pieces(output_map))
    rows = output_map.shape[1]
    head = mean_of(output_map[:, :width], mirrored[:, :width])
    tail = mean_of(output_map[:, rows - width:], mirrored[:, rows - width:])
    return mean_of(output_map, mirrored), head, tail


def body(features, w_dilated, w_pointwise, norm_gain, norm_bias):
    count, tile_rows, tile_cols = features.shape
    kernel = w_dilated[0].reshape(9, count, count)
    extended = padded(features, (("row", 1), ("col", 2)), FIRST_DILATION)
    hidden = hidden_of(
        extended, kernel, norm_gain[0, 0], norm_bias[0, 0], FIRST_DILATION, tile_rows, tile_cols
    )
    hidden = lax.optimization_barrier(hidden)
    output_map = block_output(features, hidden, norm_gain[0], norm_bias[0], w_pointwise[0])
    state, head, tail = symmetrized(output_map, SECOND_DILATION)

    kernel = w_dilated[1]
    both = jnp.concatenate([kernel, jnp.swapaxes(kernel, 0, 1)], axis=2).reshape(9, 2 * count, count)
    n_row = lax.axis_size("row")
    up = [(i, i + 1) for i in range(n_row - 1)]
    down = [(j, i) for i, j in up]
    rows = jnp.concatenate([lax.ppermute(tail, "row", up), state, lax.ppermute(head, "row", down)], axis=1)
    extended = padded(rows, (("col", 2),), SECOND_DILATION)
    gain = jnp.concatenate([norm_gain[1, 0], norm_gain[1, 0]])
    bias = jnp.concatenate([norm_bias[1, 0], norm_bias[1, 0]])
    hidden = hidden_of(extended, both, gain, bias, SECOND_DILATION, tile_rows, tile_cols)
    direct = block_output(state, hidden[:count], norm_gain[1], norm_bias[1], w_pointwise[1])
    mirrored = block_output(state, hidden[count:], norm_gain[1], norm_bias[1], w_pointwise[1])
    return mean_of(direct, mirrored)


def solution(mesh):
    in_specs = (P(None, "row", "col"), P(), P(), P(), P())
    out_specs = P(None, "row", "col")
    return jax.shard_map(body, mesh=mesh, in_specs=in_specs, out_specs=out_specs, check_vma=False)
```

```python
import jax
import jax.numpy as jnp
from jax import lax
from jax.sharding import PartitionSpec as P

FIRST_DILATION = 8
SECOND_DILATION = 16


def padded(value, sides, width):
    for axis, dim in sides:
        size, length = (lax.axis_size(axis), value.shape[dim])
        up = [(i, (i + 1) % size) for i in range(size - 1)]
        down = [(j, i) for i, j in up]
        last = lax.slice_in_dim(value, length - width, length, axis=dim)
        initial = lax.slice_in_dim(value, 0, width, axis=dim)
        before = lax.ppermute(last, axis, up)
        after = lax.ppermute(initial, axis, down)
        value = jnp.concatenate([before, value, after], axis=dim)
    return value


def hidden_of(extended_input, kernel, gain, bias, dilation_rate, tile_rows, tile_cols):
    active = jnp.maximum(extended_input, jnp.zeros((), extended_input.dtype))
    windows = [
        lax.slice(
            active,
            (0, p * dilation_rate, q * dilation_rate),
            (active.shape[0], p * dilation_rate + tile_rows, q * dilation_rate + tile_cols),
        )
        for p in range(3)
        for q in range(3)
    ]
    stacked = jnp.stack(windows, axis=0)
    spread = jnp.einsum("toc,tchw->ohw", kernel, stacked, preferred_element_type=jnp.float32)
    hidden = jnp.maximum(spread * gain[:, None, None] + bias[:, None, None], 0.0)
    return hidden.astype(jnp.bfloat16)


def block_output(current_state, hidden, gain_pair, bias_pair, pointwise):
    branch = jnp.einsum("oc,chw->ohw", pointwise, hidden, preferred_element_type=jnp.float32)
    summed = (
        current_state.astype(jnp.float32)
        + branch * gain_pair[1][:, None, None]
        + bias_pair[1][:, None, None]
    )
    return lax.reduce_precision(summed, exponent_bits=8, mantissa_bits=7).astype(jnp.bfloat16)


def mirror_pieces(output_map):
    n_col = lax.axis_size("col")
    channel_count, tile_rows, tile_cols = output_map.shape
    k = tile_cols // tile_rows
    c_lo = channel_count // n_col
    lanes = 128
    fold = lanes // tile_rows
    rows = tile_rows // fold
    t = output_map.reshape(n_col, c_lo, tile_rows, k, rows, fold)
    t = jnp.transpose(t, (0, 1, 3, 4, 5, 2)).reshape(n_col, c_lo * k * rows, lanes)
    t = lax.all_to_all(t, "col", 0, 0, tiled=True)
    t = t.reshape(n_col, c_lo, k, rows, lanes)
    t = jnp.transpose(t, (0, 2, 1, 3, 4)).reshape(n_col * k, c_lo * rows, lanes)
    t = lax.all_to_all(t, "row", 0, 0, tiled=True)
    t = t.reshape(n_col, k * c_lo * rows, lanes)
    t = lax.all_to_all(t, "col", 0, 0, tiled=True)
    t = t.reshape(n_col, k, c_lo, rows, fold, tile_rows)
    t = jnp.transpose(t, (0, 2, 3, 4, 1, 5))
    return t.reshape(channel_count, tile_rows, tile_cols)


def mean_of(a, b):
    return ((a.astype(jnp.float32) + b.astype(jnp.float32)) * 0.5).astype(jnp.bfloat16)


def symmetrized(output_map, width):
    mirrored = lax.optimization_barrier(mirror_pieces(output_map))
    rows = output_map.shape[1]
    head = mean_of(output_map[:, :width], mirrored[:, :width])
    tail = mean_of(output_map[:, rows - width:], mirrored[:, rows - width:])
    return mean_of(output_map, mirrored), head, tail


def body(features, w_dilated, w_pointwise, norm_gain, norm_bias):
    count, tile_rows, tile_cols = features.shape
    kernel = w_dilated[0].reshape(9, count, count)
    extended = padded(features, (("row", 1), ("col", 2)), FIRST_DILATION)
    hidden = hidden_of(
        extended, kernel, norm_gain[0, 0], norm_bias[0, 0], FIRST_DILATION, tile_rows, tile_cols
    )
    hidden = lax.optimization_barrier(hidden)
    output_map = block_output(features, hidden, norm_gain[0], norm_bias[0], w_pointwise[0])
    state, head, tail = symmetrized(output_map, SECOND_DILATION)

    kernel = w_dilated[1]
    both = jnp.concatenate([kernel, jnp.swapaxes(kernel, 0, 1)], axis=2).reshape(9, 2 * count, count)
    n_row = lax.axis_size("row")
    up = [(i, i + 1) for i in range(n_row - 1)]
    down = [(j, i) for i, j in up]
    above, below = lax.ppermute(tail, "row", up), lax.ppermute(head, "row", down)
    width = SECOND_DILATION
    n_col = lax.axis_size("col")
    right_of = [(i, i + 1) for i in range(n_col - 1)]
    left_of = [(j, i) for i, j in right_of]

    def columns(part):
        return jnp.concatenate([part(above), part(state), part(below)], axis=1)

    last = columns(lambda v: v[:, :, tile_cols - width:])
    initial = columns(lambda v: v[:, :, :width])
    before = lax.ppermute(last, "col", right_of)
    after = lax.ppermute(initial, "col", left_of)
    rows = jnp.concatenate([above, state, below], axis=1)
    extended = jnp.concatenate([before, rows, after], axis=2)
    gain = jnp.concatenate([norm_gain[1, 0], norm_gain[1, 0]])
    bias = jnp.concatenate([norm_bias[1, 0], norm_bias[1, 0]])
    hidden = hidden_of(extended, both, gain, bias, SECOND_DILATION, tile_rows, tile_cols)
    direct = block_output(state, hidden[:count], norm_gain[1], norm_bias[1], w_pointwise[1])
    mirrored = block_output(state, hidden[count:], norm_gain[1], norm_bias[1], w_pointwise[1])
    return mean_of(direct, mirrored)


def solution(mesh):
    in_specs = (P(None, "row", "col"), P(), P(), P(), P())
    out_specs = P(None, "row", "col")
    return jax.shard_map(body, mesh=mesh, in_specs=in_specs, out_specs=out_specs, check_vma=False)
```

```python
import jax
import jax.numpy as jnp
from jax import lax
from jax.sharding import PartitionSpec as P

FIRST_DILATION = 8
SECOND_DILATION = 16


def padded(value, sides, width):
    for axis, dim in sides:
        size, length = (lax.axis_size(axis), value.shape[dim])
        up = [(i, (i + 1) % size) for i in range(size - 1)]
        down = [(j, i) for i, j in up]
        last = lax.slice_in_dim(value, length - width, length, axis=dim)
        initial = lax.slice_in_dim(value, 0, width, axis=dim)
        before = lax.ppermute(last, axis, up)
        after = lax.ppermute(initial, axis, down)
        value = jnp.concatenate([before, value, after], axis=dim)
    return value


def hidden_of(extended_input, kernel, gain, bias, dilation_rate, tile_rows, tile_cols):
    active = jnp.maximum(extended_input, jnp.zeros((), extended_input.dtype))
    windows = [
        lax.slice(
            active,
            (0, p * dilation_rate, q * dilation_rate),
            (active.shape[0], p * dilation_rate + tile_rows, q * dilation_rate + tile_cols),
        )
        for p in range(3)
        for q in range(3)
    ]
    stacked = jnp.stack(windows, axis=0)
    spread = jnp.einsum("toc,tchw->ohw", kernel, stacked, preferred_element_type=jnp.float32)
    hidden = jnp.maximum(spread * gain[:, None, None] + bias[:, None, None], 0.0)
    return hidden.astype(jnp.bfloat16)


def block_output(current_state, hidden, gain_pair, bias_pair, pointwise):
    branch = jnp.einsum("oc,chw->ohw", pointwise, hidden, preferred_element_type=jnp.float32)
    summed = (
        current_state.astype(jnp.float32)
        + branch * gain_pair[1][:, None, None]
        + bias_pair[1][:, None, None]
    )
    return lax.reduce_precision(summed, exponent_bits=8, mantissa_bits=7).astype(jnp.bfloat16)


def mirror_pieces(output_map):
    n_col = lax.axis_size("col")
    channel_count, tile_rows, tile_cols = output_map.shape
    k = tile_cols // tile_rows
    c_lo = channel_count // n_col
    lanes = 128
    fold = lanes // tile_rows
    rows = tile_rows // fold
    t = output_map.reshape(n_col, c_lo, tile_rows, k, rows, fold)
    t = jnp.transpose(t, (0, 1, 3, 4, 5, 2)).reshape(n_col, c_lo * k * rows, lanes)
    t = lax.all_to_all(t, "col", 0, 0, tiled=True)
    t = t.reshape(n_col, c_lo, k, rows, lanes)
    t = jnp.transpose(t, (0, 2, 1, 3, 4)).reshape(n_col * k, c_lo * rows, lanes)
    t = lax.all_to_all(t, "row", 0, 0, tiled=True)
    t = t.reshape(n_col, k * c_lo * rows, lanes)
    t = lax.all_to_all(t, "col", 0, 0, tiled=True)
    t = t.reshape(n_col, k, c_lo, rows, fold, tile_rows)
    t = jnp.transpose(t, (0, 2, 3, 4, 1, 5))
    return t.reshape(channel_count, tile_rows, tile_cols)


def mean_of(a, b):
    return ((a.astype(jnp.float32) + b.astype(jnp.float32)) * 0.5).astype(jnp.bfloat16)


def symmetrized(output_map, width):
    mirrored = lax.optimization_barrier(mirror_pieces(output_map))
    rows = output_map.shape[1]
    head = mean_of(output_map[:, :width], mirrored[:, :width])
    tail = mean_of(output_map[:, rows - width:], mirrored[:, rows - width:])
    return mean_of(output_map, mirrored), head, tail


def body(features, w_dilated, w_pointwise, norm_gain, norm_bias):
    count, tile_rows, tile_cols = features.shape
    kernel = w_dilated[0].reshape(9, count, count)
    n_row = lax.axis_size("row")
    n_col = lax.axis_size("col")
    down_rows = [(i, i + 1) for i in range(n_row - 1)]
    up_rows = [(j, i) for i, j in down_rows]
    width = FIRST_DILATION
    above = lax.ppermute(features[:, tile_rows - width:], "row", down_rows)
    below = lax.ppermute(features[:, :width], "row", up_rows)

    def columns(part):
        return jnp.concatenate([part(above), part(features), part(below)], axis=1)

    right_of = [(i, i + 1) for i in range(n_col - 1)]
    left_of = [(j, i) for i, j in right_of]
    before = lax.ppermute(columns(lambda v: v[:, :, tile_cols - width:]), "col", right_of)
    after = lax.ppermute(columns(lambda v: v[:, :, :width]), "col", left_of)
    extended = jnp.concatenate(
        [before, jnp.concatenate([above, features, below], axis=1), after], axis=2
    )
    hidden = hidden_of(
        extended, kernel, norm_gain[0, 0], norm_bias[0, 0], FIRST_DILATION, tile_rows, tile_cols
    )
    hidden = lax.optimization_barrier(hidden)
    output_map = block_output(features, hidden, norm_gain[0], norm_bias[0], w_pointwise[0])
    state, head, tail = symmetrized(output_map, SECOND_DILATION)

    kernel = w_dilated[1]
    both = jnp.concatenate([kernel, jnp.swapaxes(kernel, 0, 1)], axis=2).reshape(9, 2 * count, count)
    n_row = lax.axis_size("row")
    up = [(i, i + 1) for i in range(n_row - 1)]
    down = [(j, i) for i, j in up]
    above, below = lax.ppermute(tail, "row", up), lax.ppermute(head, "row", down)
    width = SECOND_DILATION
    n_col = lax.axis_size("col")
    right_of = [(i, i + 1) for i in range(n_col - 1)]
    left_of = [(j, i) for i, j in right_of]

    def columns(part):
        return jnp.concatenate([part(above), part(state), part(below)], axis=1)

    last = columns(lambda v: v[:, :, tile_cols - width:])
    initial = columns(lambda v: v[:, :, :width])
    before = lax.ppermute(last, "col", right_of)
    after = lax.ppermute(initial, "col", left_of)
    rows = jnp.concatenate([above, state, below], axis=1)
    extended = jnp.concatenate([before, rows, after], axis=2)
    gain = jnp.concatenate([norm_gain[1, 0], norm_gain[1, 0]])
    bias = jnp.concatenate([norm_bias[1, 0], norm_bias[1, 0]])
    hidden = hidden_of(extended, both, gain, bias, SECOND_DILATION, tile_rows, tile_cols)
    direct = block_output(state, hidden[:count], norm_gain[1], norm_bias[1], w_pointwise[1])
    mirrored = block_output(state, hidden[count:], norm_gain[1], norm_bias[1], w_pointwise[1])
    return mean_of(direct, mirrored)


def solution(mesh):
    in_specs = (P(None, "row", "col"), P(), P(), P(), P())
    out_specs = P(None, "row", "col")
    return jax.shard_map(body, mesh=mesh, in_specs=in_specs, out_specs=out_specs, check_vma=False)
```

```python
import jax
import jax.numpy as jnp
from jax import lax
from jax.sharding import PartitionSpec as P

FIRST_DILATION = 8
SECOND_DILATION = 16


def padded(value, sides, width):
    for axis, dim in sides:
        size, length = (lax.axis_size(axis), value.shape[dim])
        up = [(i, (i + 1) % size) for i in range(size - 1)]
        down = [(j, i) for i, j in up]
        last = lax.slice_in_dim(value, length - width, length, axis=dim)
        initial = lax.slice_in_dim(value, 0, width, axis=dim)
        before = lax.ppermute(last, axis, up)
        after = lax.ppermute(initial, axis, down)
        value = jnp.concatenate([before, value, after], axis=dim)
    return value


def hidden_of(extended_input, kernel, gain, bias, dilation_rate, tile_rows, tile_cols):
    active = jnp.maximum(extended_input, jnp.zeros((), extended_input.dtype))
    windows = [
        lax.slice(
            active,
            (0, p * dilation_rate, q * dilation_rate),
            (active.shape[0], p * dilation_rate + tile_rows, q * dilation_rate + tile_cols),
        )
        for p in range(3)
        for q in range(3)
    ]
    stacked = jnp.stack(windows, axis=0)
    spread = jnp.einsum("toc,tchw->ohw", kernel, stacked, preferred_element_type=jnp.float32)
    hidden = jnp.maximum(spread * gain[:, None, None] + bias[:, None, None], 0.0)
    return hidden.astype(jnp.bfloat16)


def block_output(current_state, hidden, gain_pair, bias_pair, pointwise):
    branch = jnp.einsum("oc,chw->ohw", pointwise, hidden, preferred_element_type=jnp.float32)
    summed = (
        current_state.astype(jnp.float32)
        + branch * gain_pair[1][:, None, None]
        + bias_pair[1][:, None, None]
    )
    return lax.reduce_precision(summed, exponent_bits=8, mantissa_bits=7).astype(jnp.bfloat16)


def mirror_pieces(output_map):
    n_col = lax.axis_size("col")
    channel_count, tile_rows, tile_cols = output_map.shape
    k = tile_cols // tile_rows
    c_lo = channel_count // n_col
    lanes = 128
    fold = lanes // tile_rows
    rows = tile_rows // fold
    t = output_map.reshape(n_col, c_lo, tile_rows, k, rows, fold)
    t = jnp.transpose(t, (0, 1, 3, 4, 5, 2)).reshape(n_col, c_lo * k * rows, lanes)
    t = lax.all_to_all(t, "col", 0, 0, tiled=True)
    t = t.reshape(n_col, c_lo, k, rows, lanes)
    t = jnp.transpose(t, (0, 2, 1, 3, 4)).reshape(n_col * k, c_lo * rows, lanes)
    t = lax.all_to_all(t, "row", 0, 0, tiled=True)
    t = t.reshape(n_col, k * c_lo * rows, lanes)
    t = lax.all_to_all(t, "col", 0, 0, tiled=True)
    t = t.reshape(n_col, k, c_lo, rows, fold, tile_rows)
    t = jnp.transpose(t, (0, 2, 3, 4, 1, 5))
    return t.reshape(channel_count, tile_rows, tile_cols)


def mean_of(a, b):
    return ((a.astype(jnp.float32) + b.astype(jnp.float32)) * 0.5).astype(jnp.bfloat16)


def symmetrized(output_map, width):
    mirrored = lax.optimization_barrier(mirror_pieces(output_map))
    rows = output_map.shape[1]
    head = mean_of(output_map[:, :width], mirrored[:, :width])
    tail = mean_of(output_map[:, rows - width:], mirrored[:, rows - width:])
    return mean_of(output_map, mirrored), head, tail


def body(features, w_dilated, w_pointwise, norm_gain, norm_bias):
    count, tile_rows, tile_cols = features.shape
    kernel = w_dilated[0].reshape(9, count, count)
    extended = padded(features, (("row", 1), ("col", 2)), FIRST_DILATION)
    hidden = hidden_of(
        extended, kernel, norm_gain[0, 0], norm_bias[0, 0], FIRST_DILATION, tile_rows, tile_cols
    )
    kernel = w_dilated[1]
    both = jnp.concatenate([kernel, jnp.swapaxes(kernel, 0, 1)], axis=2).reshape(9, 2 * count, count)
    gain = jnp.concatenate([norm_gain[1, 0], norm_gain[1, 0]])
    bias = jnp.concatenate([norm_bias[1, 0], norm_bias[1, 0]])
    hidden, both, gain, bias = lax.optimization_barrier((hidden, both, gain, bias))
    output_map = block_output(features, hidden, norm_gain[0], norm_bias[0], w_pointwise[0])
    state, head, tail = symmetrized(output_map, SECOND_DILATION)

    n_row = lax.axis_size("row")
    up = [(i, i + 1) for i in range(n_row - 1)]
    down = [(j, i) for i, j in up]
    above, below = lax.ppermute(tail, "row", up), lax.ppermute(head, "row", down)
    width = SECOND_DILATION
    n_col = lax.axis_size("col")
    right_of = [(i, i + 1) for i in range(n_col - 1)]
    left_of = [(j, i) for i, j in right_of]

    def columns(part):
        return jnp.concatenate([part(above), part(state), part(below)], axis=1)

    last = columns(lambda v: v[:, :, tile_cols - width:])
    initial = columns(lambda v: v[:, :, :width])
    before = lax.ppermute(last, "col", right_of)
    after = lax.ppermute(initial, "col", left_of)
    rows = jnp.concatenate([above, state, below], axis=1)
    extended = jnp.concatenate([before, rows, after], axis=2)
    hidden = hidden_of(extended, both, gain, bias, SECOND_DILATION, tile_rows, tile_cols)
    direct = block_output(state, hidden[:count], norm_gain[1], norm_bias[1], w_pointwise[1])
    mirrored = block_output(state, hidden[count:], norm_gain[1], norm_bias[1], w_pointwise[1])
    return mean_of(direct, mirrored)


def solution(mesh):
    in_specs = (P(None, "row", "col"), P(), P(), P(), P())
    out_specs = P(None, "row", "col")
    return jax.shard_map(body, mesh=mesh, in_specs=in_specs, out_specs=out_specs, check_vma=False)
```
